32 devices in a mesh: wide: 8 (over z, x), narrow: 4 (over y, core).
Axes of the slice: x: 2, y: 2, z: 4, core: 2. Of those that a mesh axis runs over, the one named last changes fastest.
Arguments:
- tokens: bfloat16 [65536, 768], P(('wide', 'narrow')), may hold values from -6 to 6
- mask_count: int32 [128], P(('wide', 'narrow')), may hold values from 8 to 128, as said below
- mask_place: int32 [128, 128], P(('wide', 'narrow')), may hold values from 0 to 511, as said below
- upstream: bfloat16 [128, 128, 768], P(('wide', 'narrow')), may hold values from -6 to 6
- proj_weight: bfloat16 [768, 2304], P(('wide', 'narrow')), may hold values from -0.3125 to 0.3125
- proj_bias: bfloat16 [1536], P(('wide', 'narrow')), may hold values from -3 to 3
- out_weight: bfloat16 [768, 768], P(('wide', 'narrow')), may hold values from -0.4375 to 0.4375
- out_bias: bfloat16 [768], P(('wide', 'narrow')), may hold values from -3 to 3
- first_gain: bfloat16 [768], P(('wide', 'narrow')), may hold values from 0.25 to 1.75
- first_shift: bfloat16 [768], P(('wide', 'narrow')), may hold values from -3 to 3
- up_weight: bfloat16 [768, 3072], P(('wide', 'narrow')), may hold values from -0.21875 to 0.21875
- up_bias: bfloat16 [3072], P(('wide', 'narrow')), may hold values from -3 to 3
- down_weight: bfloat16 [3072, 768], P(('wide', 'narrow')), may hold values from -0.15625 to 0.15625
- down_bias: bfloat16 [768], P(('wide', 'narrow')), may hold values from -3 to 3
- second_gain: bfloat16 [768], P(('wide', 'narrow')), may hold values from 0.25 to 1.75
- second_shift: bfloat16 [768], P(('wide', 'narrow')), may hold values from -3 to 3
Outputs:
- masked_rows: bfloat16 [128, 128, 768], P(('wide', 'narrow'))
- row_rms: bfloat16 [128, 128], P(('wide', 'narrow'))
- token_grad: bfloat16 [65536, 768], P(('wide', 'narrow'))
- grad_proj_weight: float32 [768, 2304], P(('wide', 'narrow'))
- grad_proj_bias: float32 [1536], P(('wide', 'narrow'))
- grad_out_weight: float32 [768, 768], P(('wide', 'narrow'))
- grad_out_bias: float32 [768], P(('wide', 'narrow'))
- grad_first_gain: float32 [768], P(('wide', 'narrow'))
- grad_first_shift: float32 [768], P(('wide', 'narrow'))
- grad_up_weight: float32 [768, 3072], P(('wide', 'narrow'))
- grad_up_bias: float32 [3072], P(('wide', 'narrow'))
- grad_down_weight: float32 [3072, 768], P(('wide', 'narrow'))
- grad_down_bias: float32 [768], P(('wide', 'narrow'))
- grad_second_gain: float32 [768], P(('wide', 'narrow'))
- grad_second_shift: float32 [768], P(('wide', 'narrow'))
The draws below stay inside these ranges and needn't reach their ends.
Inputs may be any that keep to these rules, and one draw needn't show every extreme that they name: `mask_count`: sequences are numbered in device order, 4 to a device. Among the 16 sequences of the devices that share an index of wide, the counts sum to exactly 1024, and one of these devices has all its counts equal to 128. `mask_place`: the entries of a row are distinct positions of the sequence; only the first mask_count of them name masked positions.
All inputs are finite; a program needn't handle non-finite values.
Results may differ from the reference program's by a relative error of at most 0.015.
The reference program's roundings to bfloat16 on the way count: a program that leaves them out, or rounds other values in their place, can miss the bound.
Values may be sent and summed in bfloat16 or wider, within the bound.
No kernel may reach another device: no remote copies, remote signals or barrier semaphores. Data moves between devices by JAX's collectives and lax.ppermute only.
A program may use at most 192 MiB of HBM per device.

```python
import math
import jax
import jax.numpy as jnp
from jax import lax

D = 768
HEAD_DIM = 64
FF = 3072
LEN = 512
SEQ_DEV = 4
CAP = 128
SEQS = 128
TOKENS = 65536


def permute_positions(seq_key):
    return jax.random.permutation(seq_key, LEN)


def draw_mask_count(key, part):
    group_count = SEQS // (4 * SEQ_DEV)
    key_full, key_large, key_small, key_order = jax.random.split(key, 4)
    full_device = jax.random.randint(key_full, (group_count,), 0, 4)
    large_count = CAP // 2 + jax.random.randint(key_large, (group_count, SEQ_DEV), 0, CAP // 8 + 1)
    small_count = CAP // 16 + jax.random.randint(key_small, (group_count, SEQ_DEV), 0, CAP // 8 + 1)
    middle_count = CAP - large_count - small_count
    others = jnp.concatenate([large_count, middle_count, small_count], axis=1)
    order_keys = jax.random.split(key_order, group_count)
    others = jax.vmap(jax.random.permutation)(order_keys, others)
    position = jnp.arange(4 * SEQ_DEV)
    device_of = position // SEQ_DEV
    shifted = jnp.where(device_of[None, :] > full_device[:, None], position[None, :] - SEQ_DEV, position[None, :])
    shifted = jnp.clip(shifted, 0, 3 * SEQ_DEV - 1)
    picked = jnp.take_along_axis(others, shifted, axis=1)
    counts = jnp.where(device_of[None, :] == full_device[:, None], CAP, picked)
    return counts.reshape(SEQS).astype(jnp.int32)


def draw_mask_place(key, part):
    seq_keys = jax.random.split(key, SEQS)
    orders = jax.vmap(permute_positions)(seq_keys)
    return orders[:, :CAP].astype(jnp.int32)


def level_of(own_key, extent, cuts, least, high):
    loudness, own = 1.0, jax.random.fold_in(own_key, 6)
    for dim, shards_of in cuts:
        steps = jnp.exp(jax.random.uniform(jax.random.fold_in(own, dim), (shards_of,), jnp.float32, least / len(cuts), high / len(cuts)))
        loudness = loudness * jnp.repeat(steps, extent[dim] // shards_of).reshape([-1 if axis == dim else 1 for axis in range(len(extent))])
    return loudness


def gaussian(stream_key, extent, scale, limit, cuts=(), held_as=jnp.bfloat16):
    factor_of = level_of(stream_key, extent, cuts, -0.22, 0.18) if cuts else 1.0
    entries = jax.random.normal(stream_key, extent, jnp.float32) * scale * factor_of
    return jnp.minimum(jnp.maximum(entries, -limit), limit).astype(held_as)


def setup_inputs(seed: int = 0) -> dict:
    key_list = jax.random.split(jax.random.key(seed), 17)
    return {
        "tokens": gaussian(key_list[0], (TOKENS, D), 1.0, 6.0, ((0, 32),)),
        "mask_count": draw_mask_count(jax.random.fold_in(key_list[16], 71), 0),
        "mask_place": draw_mask_place(jax.random.fold_in(key_list[16], 71), 0),
        "upstream": gaussian(key_list[3], (SEQS, CAP, D), 1.0, 6.0, ((0, 32),)),
        "proj_weight": gaussian(key_list[4], (D, 3 * D), (D // 2) ** -0.5, 0.3125, ((0, 32),)),
        "proj_bias": gaussian(key_list[5], (2 * D,), 0.5, 3.0, ((0, 32),)),
        "out_weight": gaussian(key_list[6], (D, D), (D // 4) ** -0.5, 0.4375, ((0, 32),)),
        "out_bias": gaussian(key_list[7], (D,), 0.5, 3.0, ((0, 32),)),
        "first_gain": jnp.clip(1.0 + 0.15 * jax.random.normal(key_list[8], (D,), jnp.float32), 0.25, 1.75).astype(jnp.bfloat16),
        "first_shift": gaussian(key_list[9], (D,), 0.5, 3.0, ((0, 32),)),
        "up_weight": gaussian(key_list[10], (D, FF), D ** -0.5, 0.21875, ((0, 32),)),
        "up_bias": gaussian(key_list[11], (FF,), 0.5, 3.0, ((0, 32),)),
        "down_weight": gaussian(key_list[12], (FF, D), (FF // 2) ** -0.5, 0.15625, ((0, 32),)),
        "down_bias": gaussian(key_list[13], (D,), 0.5, 3.0, ((0, 32),)),
        "second_gain": jnp.clip(1.0 + 0.15 * jax.random.normal(key_list[14], (D,), jnp.float32), 0.25, 1.75).astype(jnp.bfloat16),
        "second_shift": gaussian(key_list[15], (D,), 0.5, 3.0, ((0, 32),)),
    }


@jax.custom_vjp
def low(v):
    return lax.optimization_barrier(v.astype(jnp.bfloat16)).astype(jnp.float32)

@jax.custom_vjp
def low_back(v):
    return v

def low_keep(v):
    return (low(v), None)

def low_pass(kept, grad):
    return (grad,)

def back_keep(v):
    return (v, None)

def back_low(kept, grad):
    return (low(grad),)
low.defvjp(low_keep, low_pass)
low_back.defvjp(back_keep, back_low)
norm_eps = 1e-12

def layer_norm(values, gain, shift):
    center = lax.optimization_barrier(jnp.mean(values, axis=-1, keepdims=True))
    centered = values - center
    spread = lax.optimization_barrier(jnp.mean(centered * centered, axis=-1, keepdims=True))
    return centered * lax.rsqrt(spread + norm_eps) * gain + shift

def gelu_exact(values):
    return jax.nn.gelu(values, approximate=False)

def forward(token_in, place_part, valid_part, proj_weight, proj_bias, out_weight, out_bias, first_gain, first_shift, up_weight, up_bias, down_weight, down_bias, second_gain, second_shift):
    highest = lax.Precision.HIGHEST
    model_width = token_in.shape[-1]
    head_count = model_width // HEAD_DIM
    joint_rows = jnp.einsum('gld,de->gle', token_in, proj_weight, precision=highest)
    queries = low(low_back(joint_rows[..., :model_width] + proj_bias[:model_width]))
    key_rows = low(low_back(joint_rows[..., model_width:2 * model_width]))
    values = low(low_back(joint_rows[..., 2 * model_width:] + proj_bias[model_width:]))
    head_shape = token_in.shape[:2] + (head_count, HEAD_DIM)
    scores = low_back(jnp.einsum('glhd,gmhd->ghlm', queries.reshape(head_shape), key_rows.reshape(head_shape), precision=highest) * HEAD_DIM ** (-0.5))
    probs_low = low(jax.nn.softmax(scores, axis=-1))
    context = jnp.einsum('ghlm,gmhd->glhd', probs_low, values.reshape(head_shape), precision=highest)
    context = low(low_back(context.reshape(token_in.shape)))
    attn_branch = low_back(jnp.einsum('gld,de->gle', context, out_weight, precision=highest) + out_bias)
    normed = layer_norm(token_in + attn_branch, first_gain, first_shift)
    picked = low(low_back(jnp.take_along_axis(normed, place_part[..., None], axis=1)))
    up_pre = low_back(jnp.einsum('gcd,df->gcf', picked, up_weight, precision=highest) + up_bias)
    hidden = low(gelu_exact(up_pre))
    ffn_branch = low_back(jnp.einsum('gcf,fd->gcd', hidden, down_weight, precision=highest) + down_bias)
    mixed = picked + ffn_branch
    row_rms = jnp.sqrt(lax.optimization_barrier(jnp.mean(mixed * mixed, axis=-1))) * valid_part
    masked = layer_norm(mixed, second_gain, second_shift) * valid_part[..., None]
    return (masked, row_rms)

def reference(tokens, mask_count, mask_place, upstream, proj_weight, proj_bias, out_weight, out_bias, first_gain, first_shift, up_weight, up_bias, down_weight, down_bias, second_gain, second_shift):
    seq_count = mask_count.shape[0]
    model_width = tokens.shape[1]
    length = tokens.shape[0] // seq_count
    slot_count = mask_place.shape[1]
    per_step = math.gcd(seq_count, 8)
    step_count = seq_count // per_step
    params = tuple((weight_arg.astype(jnp.float32) for weight_arg in (proj_weight, proj_bias, out_weight, out_bias, first_gain, first_shift, up_weight, up_bias, down_weight, down_bias, second_gain, second_shift)))
    is_valid = (jnp.arange(slot_count)[None, :] < mask_count[:, None]).astype(jnp.float32)
    batches = (tokens.astype(jnp.float32).reshape(step_count, per_step, length, model_width), mask_place.astype(jnp.int32).reshape(step_count, per_step, slot_count), is_valid.reshape(step_count, per_step, slot_count), upstream.astype(jnp.float32).reshape(step_count, per_step, slot_count, model_width))

    def advance(totals, batch_in):
        token_part, place_part, valid_part, upstream_part = batch_in

        def layer_fn(token_in, *weights):
            return forward(token_in, place_part, valid_part, *weights)
        masked, pullback, rms_part = jax.vjp(layer_fn, token_part, *params, has_aux=True)
        gradients = pullback(upstream_part)
        totals = tuple((running + increment for running, increment in zip(totals, gradients[1:])))
        return (totals, (masked.astype(jnp.bfloat16), rms_part.astype(jnp.bfloat16), gradients[0].astype(jnp.bfloat16)))
    starting = tuple((jnp.zeros_like(weight_arg) for weight_arg in params))
    totals, stacked = lax.scan(advance, starting, batches)
    masked_rows = stacked[0].reshape(seq_count, slot_count, model_width)
    row_rms = stacked[1].reshape(seq_count, slot_count)
    token_grad = stacked[2].reshape(seq_count * length, model_width)
    return (masked_rows, row_rms, token_grad, totals[0], totals[1], totals[2], totals[3], totals[4], totals[5], totals[6], totals[7], totals[8], totals[9], totals[10], totals[11])
```

```python
import jax
import jax.numpy as jnp
from jax import lax
from jax.sharding import PartitionSpec as P

HEAD_DIM = 64


norm_eps = 1e-12


def layer_norm(values, gain, shift):
    center = jnp.mean(values, axis=-1, keepdims=True)
    centered = values - center
    spread = jnp.mean(centered * centered, axis=-1, keepdims=True)
    return centered * lax.rsqrt(spread + norm_eps) * gain + shift


def gelu_exact(values):
    return jax.nn.gelu(values, approximate=False)


def to_pairs(matrix, seq_count):
    pair_width = 2 * HEAD_DIM
    length = matrix.shape[0] // seq_count
    return matrix.reshape(seq_count, length, matrix.shape[1] // pair_width, pair_width).transpose(
        2, 0, 1, 3
    )


def from_pairs(blocks):
    return blocks.transpose(1, 2, 0, 3).reshape(
        blocks.shape[1] * blocks.shape[2], blocks.shape[0] * blocks.shape[3]
    )


def split_heads(block_rows):
    return block_rows.reshape(block_rows.shape[0], block_rows.shape[1], 2, HEAD_DIM)


def attend(head_block):
    queries, key_rows, values = head_block
    q_heads = split_heads(queries)
    k_heads = split_heads(key_rows)
    v_heads = split_heads(values)
    scores = jnp.einsum(
        "slhd,smhd->shlm", q_heads, k_heads, preferred_element_type=jnp.float32
    ) * HEAD_DIM ** (-0.5)
    row_max = jnp.max(scores, axis=-1, keepdims=True)
    expo_terms = jnp.exp(scores - row_max)
    row_total = jnp.sum(expo_terms, axis=-1, keepdims=True)
    probs_low = (expo_terms / row_total).astype(jnp.bfloat16)
    context = jnp.einsum("shlm,smhd->slhd", probs_low, v_heads, preferred_element_type=jnp.float32)
    return (
        context.reshape(queries.shape).astype(jnp.bfloat16),
        (row_max + jnp.log(row_total))[..., 0],
    )


def attend_back(head_block):
    queries, key_rows, values, grad_context, log_total = head_block
    score_scale = HEAD_DIM ** (-0.5)
    q_heads = split_heads(queries)
    k_heads = split_heads(key_rows)
    v_heads = split_heads(values)
    g_heads = split_heads(grad_context)
    scores = (
        jnp.einsum("slhd,smhd->shlm", q_heads, k_heads, preferred_element_type=jnp.float32)
        * score_scale
    )
    probs = jnp.exp(scores - log_total[..., None])
    grad_probs = jnp.einsum("slhd,smhd->shlm", g_heads, v_heads, preferred_element_type=jnp.float32)
    grad_scores = (
        probs * (grad_probs - jnp.sum(probs * grad_probs, axis=-1, keepdims=True))
    ).astype(jnp.bfloat16)
    grad_queries = (
        jnp.einsum("shlm,smhd->slhd", grad_scores, k_heads, preferred_element_type=jnp.float32)
        * score_scale
    )
    grad_keys = (
        jnp.einsum("shlm,slhd->smhd", grad_scores, q_heads, preferred_element_type=jnp.float32)
        * score_scale
    )
    grad_values = jnp.einsum(
        "shlm,slhd->smhd", probs.astype(jnp.bfloat16), g_heads, preferred_element_type=jnp.float32
    )
    shape_out = queries.shape
    return (
        grad_queries.reshape(shape_out).astype(jnp.bfloat16),
        grad_keys.reshape(shape_out).astype(jnp.bfloat16),
        grad_values.reshape(shape_out).astype(jnp.bfloat16),
    )


AXES = ("wide", "narrow")


def gather_packed(pieces, width):
    blocks, layout = [], []
    for piece in pieces:
        if piece.ndim == 1:
            layout.append(("vec", piece.shape[0]))
            continue
        rows, cols = piece.shape
        blocks.append(piece.reshape(rows * cols // width, width))
        layout.append(("mat", rows, cols))
    vecs = [p for p in pieces if p.ndim == 1]
    if vecs:
        flat = jnp.concatenate(vecs)
        extra = -(-flat.shape[0] // width)
        flat = jnp.pad(flat, (0, extra * width - flat.shape[0]))
        blocks.append(flat.reshape(extra, width))
    packed = jnp.concatenate(blocks, axis=0)
    gathered = lax.all_gather(packed, AXES, axis=0, tiled=False)
    n = gathered.shape[0]
    out, row, vec_off = [], 0, 0
    vec_row = sum(r * c // width for kind, *rest in layout if kind == "mat" for r, c in [rest])
    for entry in layout:
        if entry[0] == "mat":
            _, rows, cols = entry
            span = rows * cols // width
            out.append(gathered[:, row : row + span].reshape(n * rows, cols))
            row += span
        else:
            size = entry[1]
            vec_block = gathered[:, vec_row:].reshape(n, -1)
            out.append(vec_block[:, vec_off : vec_off + size].reshape(n * size))
            vec_off += size
    return out


def scatter_packed(pieces, width, n):
    blocks, layout, vecs = [], [], []
    for piece in pieces:
        if piece.ndim == 1:
            layout.append(("vec", piece.shape[0] // n))
            vecs.append(piece.reshape(n, -1))
            continue
        rows, cols = piece.shape
        own = rows // n
        blocks.append(piece.reshape(n, own * cols // width, width))
        layout.append(("mat", own, cols))
    if vecs:
        flat = jnp.concatenate(vecs, axis=1)
        extra = -(-flat.shape[1] // width)
        flat = jnp.pad(flat, ((0, 0), (0, extra * width - flat.shape[1])))
        blocks.append(flat.reshape(n, extra, width))
    packed = jnp.concatenate(blocks, axis=1).astype(jnp.bfloat16)
    summed = lax.psum_scatter(packed, AXES, scatter_dimension=0, tiled=False).astype(jnp.float32)
    out, row, vec_off = [], 0, 0
    vec_row = sum(o * c // width for kind, *rest in layout if kind == "mat" for o, c in [rest])
    for entry in layout:
        if entry[0] == "mat":
            _, own, cols = entry
            span = own * cols // width
            out.append(summed[row : row + span].reshape(own, cols))
            row += span
        else:
            size = entry[1]
            out.append(summed[vec_row:].reshape(-1)[vec_off : vec_off + size])
            vec_off += size
    return out


def per_device(
    tokens,
    mask_count,
    mask_place,
    upstream,
    proj_weight,
    proj_bias,
    out_weight,
    out_bias,
    first_gain,
    first_shift,
    up_weight,
    up_bias,
    down_weight,
    down_bias,
    second_gain,
    second_shift,
):
    seq_count = mask_count.shape[0]
    model_width = tokens.shape[1]
    length = tokens.shape[0] // seq_count
    slot_count = mask_place.shape[1]
    n_dev = model_width // proj_weight.shape[0]
    (
        joint_weight,
        joint_bias,
        outer_bias,
        gain_one,
        shift_one,
        up_offset,
        down_offset,
        gain_two,
        shift_two,
    ) = gather_packed(
        (proj_weight, proj_bias, out_bias, first_gain, first_shift, up_bias, down_bias, second_gain, second_shift),
        proj_weight.shape[1],
    )
    outer_weight, up_matrix, down_matrix = gather_packed(
        (out_weight, up_weight, down_weight), model_width
    )
    joint_rows = jnp.dot(tokens, joint_weight, preferred_element_type=jnp.float32)
    queries = (joint_rows[:, :model_width] + joint_bias[:model_width]).astype(jnp.bfloat16)
    key_rows = joint_rows[:, model_width : 2 * model_width].astype(jnp.bfloat16)
    values = (joint_rows[:, 2 * model_width :] + joint_bias[model_width:]).astype(jnp.bfloat16)
    head_inputs = (
        to_pairs(queries, seq_count),
        to_pairs(key_rows, seq_count),
        to_pairs(values, seq_count),
    )
    context_pairs, log_total = lax.map(attend, head_inputs)
    context = from_pairs(context_pairs)
    resid_sum = tokens.astype(jnp.float32) + (
        jnp.dot(context, outer_weight, preferred_element_type=jnp.float32) + outer_bias
    )
    normed, first_back = jax.vjp(
        layer_norm, resid_sum, gain_one.astype(jnp.float32), shift_one.astype(jnp.float32)
    )
    gain_two = gain_two.astype(jnp.float32)
    shift_two = shift_two.astype(jnp.float32)
    is_valid = jnp.arange(slot_count)[None, :] < mask_count[:, None]
    valid_f = is_valid.astype(jnp.float32).reshape(-1)
    chooser = (mask_place[:, :, None] == jnp.arange(length)[None, None, :]).astype(jnp.bfloat16)
    normed_low = normed.astype(jnp.bfloat16).reshape(seq_count, length, model_width)
    picked = jnp.einsum(
        "scl,sld->scd", chooser, normed_low, preferred_element_type=jnp.float32
    ).astype(jnp.bfloat16).reshape(seq_count * slot_count, model_width)
    up_pre = jnp.dot(picked, up_matrix, preferred_element_type=jnp.float32) + up_offset.astype(jnp.float32)
    hidden = gelu_exact(up_pre).astype(jnp.bfloat16)
    mixed = picked.astype(jnp.float32) + (
        jnp.dot(hidden, down_matrix, preferred_element_type=jnp.float32)
        + down_offset.astype(jnp.float32)
    )
    row_rms = (jnp.sqrt(jnp.mean(mixed * mixed, axis=-1)) * valid_f).astype(jnp.bfloat16)
    ffn_out, second_back = jax.vjp(layer_norm, mixed, gain_two, shift_two)
    masked_rows = (ffn_out * valid_f[:, None]).astype(jnp.bfloat16)
    grad_out = upstream.reshape(seq_count * slot_count, model_width).astype(jnp.float32) * valid_f[:, None]
    grad_mixed, gain2_term, shift2_term = second_back(grad_out)
    grad_branch = grad_mixed.astype(jnp.bfloat16)
    down_bias_term = jnp.sum(grad_branch.astype(jnp.float32), axis=0)
    grad_hidden = jnp.einsum(
        "rd,fd->rf", grad_branch, down_matrix, preferred_element_type=jnp.float32
    )
    grad_up = jax.vjp(gelu_exact, up_pre)[1](grad_hidden)[0].astype(jnp.bfloat16)
    up_bias_term = jnp.sum(grad_up.astype(jnp.float32), axis=0)
    grad_picked = (
        grad_mixed + jnp.einsum("rf,df->rd", grad_up, up_matrix, preferred_element_type=jnp.float32)
    ).astype(jnp.bfloat16)
    up_term = jnp.einsum("rd,rf->df", picked, grad_up, preferred_element_type=jnp.float32)
    down_term = jnp.einsum("rf,rd->fd", hidden, grad_branch, preferred_element_type=jnp.float32)
    grad_normed = jnp.einsum(
        "scl,scd->sld",
        chooser,
        grad_picked.reshape(seq_count, slot_count, model_width),
        preferred_element_type=jnp.float32,
    ).reshape(seq_count * length, model_width)
    grad_resid, gain_one_term, shift_one_term = first_back(grad_normed)
    grad_attn = grad_resid.astype(jnp.bfloat16)
    outer_bias_term = jnp.sum(grad_attn.astype(jnp.float32), axis=0)
    outer_term = jnp.einsum("td,te->de", context, grad_attn, preferred_element_type=jnp.float32)
    (
        grad_out_weight,
        grad_up_weight,
        grad_down_weight,
        grad_out_bias,
        grad_first_gain,
        grad_first_shift,
        grad_up_bias,
        grad_down_bias,
        grad_second_gain,
        grad_second_shift,
    ) = scatter_packed(
        (
            outer_term,
            up_term,
            down_term,
            outer_bias_term,
            gain_one_term,
            shift_one_term,
            up_bias_term,
            down_bias_term,
            gain2_term,
            shift2_term,
        ),
        model_width,
        n_dev,
    )
    grad_context = jnp.einsum(
        "te,de->td", grad_attn, outer_weight, preferred_element_type=jnp.float32
    ).astype(jnp.bfloat16)
    pair_grads = lax.map(attend_back, head_inputs + (to_pairs(grad_context, seq_count), log_total))
    grad_joint = jnp.concatenate(
        [from_pairs(pair_grads[0]), from_pairs(pair_grads[1]), from_pairs(pair_grads[2])], axis=1
    )
    joint_bias_term = jnp.concatenate(
        [
            jnp.sum(grad_joint[:, :model_width].astype(jnp.float32), axis=0),
            jnp.sum(grad_joint[:, 2 * model_width :].astype(jnp.float32), axis=0),
        ]
    )
    joint_term = jnp.einsum("td,te->de", tokens, grad_joint, preferred_element_type=jnp.float32)
    grad_proj_weight, grad_proj_bias = scatter_packed(
        (joint_term, joint_bias_term), joint_term.shape[1], n_dev
    )
    token_grad = (
        grad_resid
        + jnp.einsum("te,de->td", grad_joint, joint_weight, preferred_element_type=jnp.float32)
    ).astype(jnp.bfloat16)
    return (
        masked_rows.reshape(seq_count, slot_count, model_width),
        row_rms.reshape(seq_count, slot_count),
        token_grad,
        grad_proj_weight,
        grad_proj_bias,
        grad_out_weight,
        grad_out_bias,
        grad_first_gain,
        grad_first_shift,
        grad_up_weight,
        grad_up_bias,
        grad_down_weight,
        grad_down_bias,
        grad_second_gain,
        grad_second_shift,
    )


def solution(mesh):
    placed = (
        P(("wide", "narrow"), None),
        P(("wide", "narrow")),
        P(("wide", "narrow"), None),
        P(("wide", "narrow"), None, None),
        P(("wide", "narrow"), None),
        P(("wide", "narrow")),
        P(("wide", "narrow"), None),
        P(("wide", "narrow")),
        P(("wide", "narrow")),
        P(("wide", "narrow")),
        P(("wide", "narrow"), None),
        P(("wide", "narrow")),
        P(("wide", "narrow"), None),
        P(("wide", "narrow")),
        P(("wide", "narrow")),
        P(("wide", "narrow")),
    )
    return jax.shard_map(
        per_device,
        mesh=mesh,
        in_specs=placed,
        out_specs=(
            P(("wide", "narrow"), None, None),
            P(("wide", "narrow"), None),
            P(("wide", "narrow"), None),
            P(("wide", "narrow"), None),
            P(("wide", "narrow")),
            P(("wide", "narrow"), None),
            P(("wide", "narrow")),
            P(("wide", "narrow")),
            P(("wide", "narrow")),
            P(("wide", "narrow"), None),
            P(("wide", "narrow")),
            P(("wide", "narrow"), None),
            P(("wide", "narrow")),
            P(("wide", "narrow")),
            P(("wide", "narrow")),
        ),
        check_vma=False,
    )
```
